256 devices in a mesh: layer: 2 (over core), feat: 4 (over x), tok: 32 (over z, y).
Axes of the slice: x: 4, y: 4, z: 8, core: 2. Of those that a mesh axis runs over, the one named last changes fastest.
Arguments:
- resid_in: bfloat16 [8192, 2304], P('tok', 'feat'), may hold values from -6 to 6
- attn_out: bfloat16 [2, 8192, 2304], P('layer', 'tok', 'feat'), may hold values from -4 to 4
- carry_in: bfloat16 [8192, 2304], P('tok', 'feat'), may hold values from -4 to 4
- enc_weight: bfloat16 [2, 2304, 8192], P('layer', None, 'feat'), may hold values from -0.125 to 0.125
- enc_bias: float32 [2, 8192], P('layer', 'feat'), may hold values from -3 to 3
- dec_own: bfloat16 [2, 8192, 2304], P('layer', 'feat', 'tok'), may hold values from -0.125 to 0.125
- dec_next: bfloat16 [2, 8192, 2304], P('layer', 'feat', 'tok'), may hold values from -0.125 to 0.125
- block_list: int32 [2, 64, 32], P('layer', 'tok'), may hold values from 0 to 63, all different within a row
- block_count: int32 [2, 64], P('layer', 'tok'), may hold values from 8 to 32, as said below
Outputs:
- reconstruction: bfloat16 [2, 8192, 2304], P('layer', 'tok', 'feat')
- outgoing: bfloat16 [2, 8192, 2304], P('layer', 'tok', 'feat')
The draws below stay inside these ranges and needn't reach their ends.
Inputs may be any that keep to these rules, and one draw needn't show every extreme that they name: Each row of block_list names 32 different blocks; only its first block_count entries are in use. `block_count`: some entry equals 32.
All inputs are finite; a program needn't handle non-finite values.
Results may differ from the reference program's by a relative error of at most 0.015.
Values may be sent and summed in bfloat16 or wider, within the bound.
No kernel may reach another device: no remote copies, remote signals or barrier semaphores. Data moves between devices by JAX's collectives and lax.ppermute only.
A program may use at most 128 MiB of HBM per device.

```python
import jax
import jax.numpy as jnp
from jax import lax

D = 2304
FEATURES = 8192
BLOCK = 128
TILE = 128
KMAX = 32
TILES_DEV = 2
LAYERS = 2
TILES = 64
TOKENS = 8192
BLK = 64
FEAT_DEV = 2048
N_FEAT = 4
N_TOK = 32


def draw_block_count(key, part):
    key_counts, key_spot = jax.random.split(jax.random.fold_in(key, 17))
    counts = jax.random.randint(key_counts, (LAYERS * TILES,), KMAX // 4, KMAX + 1, dtype=jnp.int32)
    position = jax.random.randint(key_spot, (), 0, LAYERS * TILES, dtype=jnp.int32)
    flattened = counts.at[position].set(KMAX)
    return flattened.reshape(LAYERS, TILES).astype(jnp.int32)


def steps_of(own_key, extent, shards, smallest, top_value):
    def one(dim, parts):
        draws = jax.random.uniform(jax.random.fold_in(jax.random.fold_in(own_key, 6), dim), (parts,), jnp.float32, smallest / len(shards), top_value / len(shards))
        return jnp.repeat(jnp.exp(draws), extent[dim] // parts).reshape((-1,) + (1,) * (len(extent) - dim - 1))

    loudness = one(*shards[0])
    for cut in shards[1:]:
        loudness = loudness * one(*cut)
    return loudness


def choose_distinct(rng, rows, number_of, top, lift):
    ranking = jax.random.permutation(jax.random.fold_in(rng, 1), number_of)
    favour = ranking
    for power in range(3):
        favour = favour * favour // number_of
    favour = favour * lift // number_of
    chance = jax.random.randint(jax.random.fold_in(rng, 2), (rows, number_of), 0, 4096) + favour
    sure = jax.random.permutation(jax.random.fold_in(rng, 3), rows)[jnp.arange(number_of) % rows]
    chance = jnp.where(jnp.arange(rows)[:, None] == sure[None, :], 1 << 14, chance)
    priority = chance * number_of + jnp.arange(number_of)
    return lax.top_k(priority.astype(jnp.int32), top)[1].astype(jnp.int32)


def gaussian(rng, extent, deviation, reach, pieces=(), held_as=jnp.bfloat16):
    array = deviation * jax.random.normal(rng, extent, jnp.float32)
    if pieces:
        array = array * steps_of(rng, extent, pieces, -0.22, 0.18)
    return jnp.clip(array, -reach, reach).astype(held_as)


def setup_inputs(seed: int = 0) -> dict:
    keys = jax.random.split(jax.random.key(seed), 10)
    return {
        "resid_in": gaussian(keys[0], (TOKENS, D), 1.0, 6.0, ((0, 32), (1, 4))),
        "attn_out": gaussian(keys[1], (LAYERS, TOKENS, D), 0.5, 4.0, ((0, 2), (1, 32), (2, 4))),
        "carry_in": gaussian(keys[2], (TOKENS, D), 0.5, 4.0, ((0, 32), (1, 4))),
        "enc_weight": gaussian(keys[3], (LAYERS, D, FEATURES), D ** -0.5, 0.125, ((0, 2), (2, 4))),
        "enc_bias": gaussian(keys[4], (LAYERS, FEATURES), 0.5, 3.0, ((0, 2), (1, 4)), jnp.float32),
        "dec_own": gaussian(keys[5], (LAYERS, FEATURES, D), (FEATURES // 4) ** -0.5, 0.125, ((0, 2), (1, 4), (2, 32))),
        "dec_next": gaussian(keys[6], (LAYERS, FEATURES, D), (FEATURES // 4) ** -0.5, 0.125, ((0, 2), (1, 4), (2, 32))),
        "block_list": choose_distinct(keys[7], LAYERS * TILES, BLK, KMAX, 8192).reshape((LAYERS, TILES, KMAX)),
        "block_count": draw_block_count(jax.random.fold_in(keys[9], 71), 0),
    }


def reference(resid_in, attn_out, carry_in, enc_weight, enc_bias, dec_own, dec_next, block_list, block_count):
    tile_total = TILES_DEV * N_TOK
    slot_ids = jnp.arange(KMAX, dtype=jnp.int32)
    block_ids = jnp.arange(BLK, dtype=jnp.int32)
    residual = resid_in
    incoming = carry_in
    recon_list = []
    outgoing_list = []
    for layer_index in range(LAYERS):
        in_use = slot_ids[None, :] < block_count[layer_index][:, None]
        matches = (block_list[layer_index][:, :, None] == block_ids[None, None, :]) & in_use[:, :, None]
        active = jnp.any(matches, axis=1).astype(jnp.float32)
        preact = jnp.dot(residual, enc_weight[layer_index], preferred_element_type=jnp.float32) + enc_bias[layer_index][None, :]
        preact = preact.reshape(tile_total, TILE, BLK, BLOCK)
        features = (jax.nn.relu(preact) * active[:, None, :, None]).reshape(tile_total * TILE, FEATURES).astype(jnp.bfloat16)
        own_part = jnp.zeros((tile_total * TILE, D), jnp.float32)
        next_part = jnp.zeros((tile_total * TILE, D), jnp.float32)
        for range_index in range(N_FEAT):
            low = range_index * FEAT_DEV
            feature_range = features[:, low:low + FEAT_DEV]
            own_term = jnp.dot(feature_range, dec_own[layer_index, low:low + FEAT_DEV], preferred_element_type=jnp.float32).astype(jnp.bfloat16)
            next_term = jnp.dot(feature_range, dec_next[layer_index, low:low + FEAT_DEV], preferred_element_type=jnp.float32).astype(jnp.bfloat16)
            own_term, next_term = lax.optimization_barrier((own_term, next_term))
            own_part = own_part + own_term.astype(jnp.float32)
            next_part = next_part + next_term.astype(jnp.float32)
        outgoing_now = next_part.astype(jnp.bfloat16)
        recon_now = own_part + incoming.astype(jnp.float32)
        residual = (residual.astype(jnp.float32) + attn_out[layer_index].astype(jnp.float32) + recon_now).astype(jnp.bfloat16)
        recon_list.append(recon_now.astype(jnp.bfloat16))
        outgoing_list.append(outgoing_now)
        incoming = outgoing_now
    return jnp.stack(recon_list), jnp.stack(outgoing_list)
```

```python
import jax
import jax.numpy as jnp
from jax import lax
from jax.sharding import PartitionSpec as P

BLOCK = 128
TILE = 128
GROUP = ("layer", "feat")


def within_layer(shard, section, shift, n_feat):
    pairs = [
        (section * n_feat + i, section * n_feat + (i + shift) % n_feat) for i in range(n_feat)
    ]
    return lax.ppermute(shard, GROUP, pairs)


def feat_gather(part, section, feat_index, n_feat):
    received = [part] + [within_layer(part, section, k, n_feat) for k in range(1, n_feat)]
    blocks = []
    for j in range(n_feat):
        block = jnp.zeros_like(part)
        for k in range(n_feat):
            block = jnp.where((feat_index - k) % n_feat == j, received[k], block)
        blocks.append(block)
    return jnp.concatenate(blocks, axis=-1)


def feat_reduce_scatter(terms, section, feat_index, n_feat):
    cols = terms.shape[-1] // n_feat
    total = lax.dynamic_slice_in_dim(terms, feat_index * cols, cols, terms.ndim - 1).astype(
        jnp.float32
    )
    for k in range(1, n_feat):
        target = (feat_index + k) % n_feat
        piece = lax.dynamic_slice_in_dim(terms, target * cols, cols, terms.ndim - 1)
        total = total + within_layer(piece, section, k, n_feat).astype(jnp.float32)
    return total


def feature_mask(block_list, block_count, feat_index, blocks_dev):
    listed = block_list[0]
    in_use = jnp.arange(listed.shape[1], dtype=jnp.int32)[None, :] < block_count[0][:, None]
    own_blocks = feat_index * blocks_dev + jnp.arange(blocks_dev, dtype=jnp.int32)
    matches = (listed[:, None, :] == own_blocks[None, :, None]) & in_use[:, None, :]
    active = jnp.any(matches, axis=2).astype(jnp.float32)
    return jnp.repeat(jnp.repeat(active, TILE, axis=0), BLOCK, axis=1)


def decode_every(gathered, enc_weight, enc_bias, decoders, mask):
    preact = (
        jnp.dot(gathered, enc_weight[0], preferred_element_type=jnp.float32) + enc_bias[0][None, :]
    )
    features = (jax.nn.relu(preact) * mask).astype(jnp.bfloat16)
    own_part = jnp.dot(features, decoders[0], preferred_element_type=jnp.float32)
    next_part = jnp.dot(features, decoders[1], preferred_element_type=jnp.float32)
    return jnp.stack([own_part, next_part]).astype(jnp.bfloat16)


def shards(
    resid_in, attn_out, carry_in, enc_weight, enc_bias, dec_own, dec_next, block_list, block_count
):
    layer_count = lax.axis_size("layer")
    n_feat = lax.axis_size("feat")
    section_index = lax.axis_index("layer")
    feat_index = lax.axis_index("feat")
    blocks_dev = enc_weight.shape[2] // BLOCK
    decoders = (
        lax.all_gather(dec_own[0], "tok", axis=1, tiled=True),
        lax.all_gather(dec_next[0], "tok", axis=1, tiled=True),
    )
    mask = feature_mask(block_list, block_count, feat_index, blocks_dev)
    attention = attn_out[0].astype(jnp.float32)

    residual = resid_in
    incoming = carry_in
    recon_out = jnp.zeros_like(resid_in)
    outgoing_out = jnp.zeros_like(resid_in)
    for section in range(layer_count):
        gathered = feat_gather(residual, section, feat_index, n_feat)
        terms = lax.cond(
            section_index == section,
            lambda source: decode_every(source, enc_weight, enc_bias, decoders, mask),
            lambda source: jnp.zeros((2,) + source.shape, jnp.bfloat16),
            gathered,
        )
        summed = feat_reduce_scatter(terms, section, feat_index, n_feat)
        recon_now = summed[0] + incoming.astype(jnp.float32)
        new_residual = (residual.astype(jnp.float32) + attention + recon_now).astype(jnp.bfloat16)
        outgoing_now = summed[1].astype(jnp.bfloat16)
        here = section_index == section
        recon_out = jnp.where(here, recon_now.astype(jnp.bfloat16), recon_out)
        outgoing_out = jnp.where(here, outgoing_now, outgoing_out)
        if section + 1 < layer_count:
            arrived = lax.ppermute(
                jnp.stack([new_residual, outgoing_now]), "layer", [(section, section + 1)]
            )
            residual = arrived[0]
            incoming = arrived[1]
    return (recon_out[None], outgoing_out[None])


def solution(mesh):
    return jax.shard_map(
        shards,
        mesh=mesh,
        in_specs=(
            P("tok", "feat"),
            P("layer", "tok", "feat"),
            P("tok", "feat"),
            P("layer", None, "feat"),
            P("layer", "feat"),
            P("layer", "feat", "tok"),
            P("layer", "feat", "tok"),
            P("layer", "tok", None),
            P("layer", "tok"),
        ),
        out_specs=(P("layer", "tok", "feat"), P("layer", "tok", "feat")),
        check_vma=False,
    )
```

```python
import jax
import jax.numpy as jnp
from jax import lax
from jax.sharding import PartitionSpec as P

BLOCK = 128
TILE = 128
GROUP = ("layer", "feat")


def within_layer(shard, section, shift, n_feat):
    if section is None:
        return lax.ppermute(shard, "feat", [(i, (i + shift) % n_feat) for i in range(n_feat)])
    pairs = [
        (section * n_feat + i, section * n_feat + (i + shift) % n_feat) for i in range(n_feat)
    ]
    return lax.ppermute(shard, GROUP, pairs)


def feat_gather(part, section, feat_index, n_feat):
    received = [part] + [within_layer(part, section, k, n_feat) for k in range(1, n_feat)]
    blocks = []
    for j in range(n_feat):
        block = jnp.zeros_like(part)
        for k in range(n_feat):
            block = jnp.where((feat_index - k) % n_feat == j, received[k], block)
        blocks.append(block)
    return jnp.concatenate(blocks, axis=-1)


def feat_reduce_scatter(terms, section, feat_index, n_feat):
    cols = terms.shape[-1] // n_feat
    total = lax.dynamic_slice_in_dim(terms, feat_index * cols, cols, terms.ndim - 1).astype(
        jnp.float32
    )
    for k in range(1, n_feat):
        target = (feat_index + k) % n_feat
        piece = lax.dynamic_slice_in_dim(terms, target * cols, cols, terms.ndim - 1)
        total = total + within_layer(piece, section, k, n_feat).astype(jnp.float32)
    return total


def feature_mask(block_list, block_count, feat_index, blocks_dev):
    listed = block_list[0]
    in_use = jnp.arange(listed.shape[1], dtype=jnp.int32)[None, :] < block_count[0][:, None]
    own_blocks = feat_index * blocks_dev + jnp.arange(blocks_dev, dtype=jnp.int32)
    matches = (listed[:, None, :] == own_blocks[None, :, None]) & in_use[:, None, :]
    active = jnp.any(matches, axis=2).astype(jnp.float32)
    return jnp.repeat(jnp.repeat(active, TILE, axis=0), BLOCK, axis=1)


def encode(gathered, enc_weight, enc_bias, mask):
    preact = (
        jnp.dot(gathered, enc_weight[0], preferred_element_type=jnp.float32) + enc_bias[0][None, :]
    )
    return (jax.nn.relu(preact) * mask).astype(jnp.bfloat16)


def shards(
    resid_in, attn_out, carry_in, enc_weight, enc_bias, dec_own, dec_next, block_list, block_count
):
    n_feat = lax.axis_size("feat")
    section_index = lax.axis_index("layer")
    feat_index = lax.axis_index("feat")
    blocks_dev = enc_weight.shape[2] // BLOCK
    first_core = section_index == 0
    first_dec = jnp.where(first_core, dec_own[0], lax.ppermute(dec_next[0], "layer", [(0, 1)]))
    second_dec = jnp.where(first_core, lax.ppermute(dec_next[0], "layer", [(1, 0)]), dec_own[0])
    first_full = lax.all_gather(first_dec, "tok", axis=1, tiled=True)
    second_full = lax.all_gather(second_dec, "tok", axis=1, tiled=True)
    mask = feature_mask(block_list, block_count, feat_index, blocks_dev)
    attention = attn_out[0].astype(jnp.float32)

    gathered = feat_gather(resid_in, 0, feat_index, n_feat)
    features = lax.cond(
        first_core,
        lambda source: encode(source, enc_weight, enc_bias, mask),
        lambda source: jnp.zeros((source.shape[0], enc_weight.shape[2]), jnp.bfloat16),
        gathered,
    )
    features = jnp.where(first_core, features, lax.ppermute(features, "layer", [(0, 1)]))
    part = jnp.dot(features, first_full, preferred_element_type=jnp.float32).astype(jnp.bfloat16)
    summed = feat_reduce_scatter(part, None, feat_index, n_feat)
    recon_first = summed + carry_in.astype(jnp.float32)
    residual_next = (resid_in.astype(jnp.float32) + attention + recon_first).astype(jnp.bfloat16)
    outgoing_first = summed.astype(jnp.bfloat16)
    swapped = lax.ppermute(
        jnp.where(first_core, residual_next, outgoing_first), "layer", [(0, 1), (1, 0)]
    )

    gathered = feat_gather(swapped, 1, feat_index, n_feat)
    features = lax.cond(
        first_core,
        lambda source: jnp.zeros((source.shape[0], enc_weight.shape[2]), jnp.bfloat16),
        lambda source: encode(source, enc_weight, enc_bias, mask),
        gathered,
    )
    features = jnp.where(first_core, lax.ppermute(features, "layer", [(1, 0)]), features)
    part = jnp.dot(features, second_full, preferred_element_type=jnp.float32).astype(jnp.bfloat16)
    summed = feat_reduce_scatter(part, None, feat_index, n_feat)
    recon_second = summed + outgoing_first.astype(jnp.float32)
    outgoing_second = lax.ppermute(summed.astype(jnp.bfloat16), "layer", [(0, 1)])

    recon_out = jnp.where(first_core, recon_first, recon_second).astype(jnp.bfloat16)
    outgoing_out = jnp.where(first_core, swapped, outgoing_second)
    return (recon_out[None], outgoing_out[None])


def solution(mesh):
    return jax.shard_map(
        shards,
        mesh=mesh,
        in_specs=(
            P("tok", "feat"),
            P("layer", "tok", "feat"),
            P("tok", "feat"),
            P("layer", None, "feat"),
            P("layer", "feat"),
            P("layer", "feat", "tok"),
            P("layer", "feat", "tok"),
            P("layer", "tok", None),
            P("layer", "tok"),
        ),
        out_specs=(P("layer", "tok", "feat"), P("layer", "tok", "feat")),
        check_vma=False,
    )
```

```python
import jax
import jax.numpy as jnp
from jax import lax
from jax.sharding import PartitionSpec as P

BLOCK = 128
TILE = 128
GROUP = ("layer", "feat")
SPLIT = 1024


def within_layer(shard, section, shift, n_feat):
    if section is None:
        return lax.ppermute(shard, "feat", [(i, (i + shift) % n_feat) for i in range(n_feat)])
    pairs = [
        (section * n_feat + i, section * n_feat + (i + shift) % n_feat) for i in range(n_feat)
    ]
    return lax.ppermute(shard, GROUP, pairs)


def feat_gather(part, section, feat_index, n_feat):
    received = [part] + [within_layer(part, section, k, n_feat) for k in range(1, n_feat)]
    blocks = []
    for j in range(n_feat):
        block = jnp.zeros_like(part)
        for k in range(n_feat):
            block = jnp.where((feat_index - k) % n_feat == j, received[k], block)
        blocks.append(block)
    return jnp.concatenate(blocks, axis=-1)


def feat_reduce_scatter(terms, section, feat_index, n_feat):
    cols = terms.shape[-1] // n_feat
    total = lax.dynamic_slice_in_dim(terms, feat_index * cols, cols, terms.ndim - 1).astype(
        jnp.float32
    )
    for k in range(1, n_feat):
        target = (feat_index + k) % n_feat
        piece = lax.dynamic_slice_in_dim(terms, target * cols, cols, terms.ndim - 1)
        total = total + within_layer(piece, section, k, n_feat).astype(jnp.float32)
    return total


def feature_mask(block_list, block_count, feat_index, blocks_dev):
    listed = block_list[0]
    in_use = jnp.arange(listed.shape[1], dtype=jnp.int32)[None, :] < block_count[0][:, None]
    own_blocks = feat_index * blocks_dev + jnp.arange(blocks_dev, dtype=jnp.int32)
    matches = (listed[:, None, :] == own_blocks[None, :, None]) & in_use[:, None, :]
    active = jnp.any(matches, axis=2).astype(jnp.float32)
    return jnp.repeat(jnp.repeat(active, TILE, axis=0), BLOCK, axis=1)


def encode(gathered, enc_weight, enc_bias, mask):
    preact = (
        jnp.dot(gathered, enc_weight[0], preferred_element_type=jnp.float32) + enc_bias[0][None, :]
    )
    return (jax.nn.relu(preact) * mask).astype(jnp.bfloat16)


def gather_columns(shard):
    n_tok = lax.axis_size("tok")
    by_gather = lax.all_gather(shard[:SPLIT], "tok", axis=1, tiled=True)
    rest = jnp.broadcast_to(shard[SPLIT:][None], (n_tok,) + shard[SPLIT:].shape)
    by_all_to_all = lax.all_to_all(rest, "tok", 0, 0, tiled=True)
    return by_gather, by_all_to_all


def decode(features, full):
    by_gather, by_all_to_all = full
    first = jnp.dot(features[:, :SPLIT], by_gather, preferred_element_type=jnp.float32)
    second = jnp.einsum(
        "tf,jfc->tjc", features[:, SPLIT:], by_all_to_all, preferred_element_type=jnp.float32
    )
    return (first + second.reshape(first.shape)).astype(jnp.bfloat16)


def shards(
    resid_in, attn_out, carry_in, enc_weight, enc_bias, dec_own, dec_next, block_list, block_count
):
    n_feat = lax.axis_size("feat")
    section_index = lax.axis_index("layer")
    feat_index = lax.axis_index("feat")
    blocks_dev = enc_weight.shape[2] // BLOCK
    first_core = section_index == 0
    first_dec = jnp.where(first_core, dec_own[0], lax.ppermute(dec_next[0], "layer", [(0, 1)]))
    second_dec = jnp.where(first_core, lax.ppermute(dec_next[0], "layer", [(1, 0)]), dec_own[0])
    first_full = gather_columns(first_dec)
    second_full = gather_columns(second_dec)
    mask = feature_mask(block_list, block_count, feat_index, blocks_dev)
    attention = attn_out[0].astype(jnp.float32)

    gathered = feat_gather(resid_in, 0, feat_index, n_feat)
    features = lax.cond(
        first_core,
        lambda source: encode(source, enc_weight, enc_bias, mask),
        lambda source: jnp.zeros((source.shape[0], enc_weight.shape[2]), jnp.bfloat16),
        gathered,
    )
    features = jnp.where(first_core, features, lax.ppermute(features, "layer", [(0, 1)]))
    part = decode(features, first_full)
    summed = feat_reduce_scatter(part, None, feat_index, n_feat)
    recon_first = summed + carry_in.astype(jnp.float32)
    residual_next = (resid_in.astype(jnp.float32) + attention + recon_first).astype(jnp.bfloat16)
    outgoing_first = summed.astype(jnp.bfloat16)
    swapped = lax.ppermute(
        jnp.where(first_core, residual_next, outgoing_first), "layer", [(0, 1), (1, 0)]
    )

    gathered = feat_gather(swapped, 1, feat_index, n_feat)
    features = lax.cond(
        first_core,
        lambda source: jnp.zeros((source.shape[0], enc_weight.shape[2]), jnp.bfloat16),
        lambda source: encode(source, enc_weight, enc_bias, mask),
        gathered,
    )
    features = jnp.where(first_core, lax.ppermute(features, "layer", [(1, 0)]), features)
    part = decode(features, second_full)
    summed = feat_reduce_scatter(part, None, feat_index, n_feat)
    recon_second = summed + outgoing_first.astype(jnp.float32)
    outgoing_second = lax.ppermute(summed.astype(jnp.bfloat16), "layer", [(0, 1)])

    recon_out = jnp.where(first_core, recon_first, recon_second).astype(jnp.bfloat16)
    outgoing_out = jnp.where(first_core, swapped, outgoing_second)
    return (recon_out[None], outgoing_out[None])


def solution(mesh):
    return jax.shard_map(
        shards,
        mesh=mesh,
        in_specs=(
            P("tok", "feat"),
            P("layer", "tok", "feat"),
            P("tok", "feat"),
            P("layer", None, "feat"),
            P("layer", "feat"),
            P("layer", "feat", "tok"),
            P("layer", "feat", "tok"),
            P("layer", "tok", None),
            P("layer", "tok"),
        ),
        out_specs=(P("layer", "tok", "feat"), P("layer", "tok", "feat")),
        check_vma=False,
    )
```

```python
import jax
import jax.numpy as jnp
from jax import lax
from jax.sharding import Mesh, PartitionSpec as P

BLOCK = 128
TILE = 128
GROUP = ("layer", "feat")
SPLIT = 1024
TOK = ("tz", "ty")


def within_layer(shard, section, shift, n_feat):
    if section is None:
        return lax.ppermute(shard, "feat", [(i, (i + shift) % n_feat) for i in range(n_feat)])
    pairs = [
        (section * n_feat + i, section * n_feat + (i + shift) % n_feat) for i in range(n_feat)
    ]
    return lax.ppermute(shard, GROUP, pairs)


def feat_gather(part, section, feat_index, n_feat):
    received = [part] + [within_layer(part, section, k, n_feat) for k in range(1, n_feat)]
    blocks = []
    for j in range(n_feat):
        block = jnp.zeros_like(part)
        for k in range(n_feat):
            block = jnp.where((feat_index - k) % n_feat == j, received[k], block)
        blocks.append(block)
    return jnp.concatenate(blocks, axis=-1)


def feat_reduce_scatter(terms, section, feat_index, n_feat):
    cols = terms.shape[-1] // n_feat
    total = lax.dynamic_slice_in_dim(terms, feat_index * cols, cols, terms.ndim - 1).astype(
        jnp.float32
    )
    for k in range(1, n_feat):
        target = (feat_index + k) % n_feat
        piece = lax.dynamic_slice_in_dim(terms, target * cols, cols, terms.ndim - 1)
        total = total + within_layer(piece, section, k, n_feat).astype(jnp.float32)
    return total


def feature_mask(block_list, block_count, feat_index, blocks_dev):
    listed = block_list[0]
    in_use = jnp.arange(listed.shape[1], dtype=jnp.int32)[None, :] < block_count[0][:, None]
    own_blocks = feat_index * blocks_dev + jnp.arange(blocks_dev, dtype=jnp.int32)
    matches = (listed[:, None, :] == own_blocks[None, :, None]) & in_use[:, None, :]
    active = jnp.any(matches, axis=2).astype(jnp.float32)
    return jnp.repeat(jnp.repeat(active, TILE, axis=0), BLOCK, axis=1)


def encode(gathered, enc_weight, enc_bias, mask):
    preact = (
        jnp.dot(gathered, enc_weight[0], preferred_element_type=jnp.float32) + enc_bias[0][None, :]
    )
    return (jax.nn.relu(preact) * mask).astype(jnp.bfloat16)


def gather_columns(shard):
    n_y = lax.axis_size("ty")
    y_index = lax.axis_index("ty")
    by_gather = lax.all_gather(shard[:SPLIT], TOK, axis=1, tiled=True)
    along_z = lax.all_gather(shard[SPLIT:], "tz", axis=0)
    received = [along_z] + [
        lax.ppermute(along_z, "ty", [(i, (i + k) % n_y) for i in range(n_y)]) for k in range(1, n_y)
    ]
    blocks = []
    for j in range(n_y):
        block = jnp.zeros_like(along_z)
        for k in range(n_y):
            block = jnp.where((y_index - k) % n_y == j, received[k], block)
        blocks.append(block)
    return by_gather, jnp.stack(blocks, axis=1)


def decode(features, full):
    by_gather, by_rest = full
    first = jnp.dot(features[:, :SPLIT], by_gather, preferred_element_type=jnp.float32)
    second = jnp.einsum(
        "tf,zyfc->tzyc", features[:, SPLIT:], by_rest, preferred_element_type=jnp.float32
    )
    return (first + second.reshape(first.shape)).astype(jnp.bfloat16)


def shards(
    resid_in, attn_out, carry_in, enc_weight, enc_bias, dec_own, dec_next, block_list, block_count
):
    n_feat = lax.axis_size("feat")
    section_index = lax.axis_index("layer")
    feat_index = lax.axis_index("feat")
    blocks_dev = enc_weight.shape[2] // BLOCK
    first_core = section_index == 0
    own_full = gather_columns(dec_own[0])
    next_full = gather_columns(dec_next[0])
    mask = feature_mask(block_list, block_count, feat_index, blocks_dev)
    attention = attn_out[0].astype(jnp.float32)

    def encoded(source, section):
        return lax.cond(
            section_index == section,
            lambda inner: encode(inner, enc_weight, enc_bias, mask),
            lambda inner: jnp.zeros((inner.shape[0], enc_weight.shape[2]), jnp.bfloat16),
            source,
        )

    features_first = encoded(feat_gather(resid_in, 0, feat_index, n_feat), 0)
    own_first = feat_reduce_scatter(decode(features_first, own_full), 0, feat_index, n_feat)
    recon_first = own_first + carry_in.astype(jnp.float32)
    residual_next = (resid_in.astype(jnp.float32) + attention + recon_first).astype(jnp.bfloat16)
    residual_next = lax.ppermute(residual_next, "layer", [(0, 1)])

    features_second = encoded(feat_gather(residual_next, 1, feat_index, n_feat), 1)
    own_second = feat_reduce_scatter(decode(features_second, own_full), 1, feat_index, n_feat)

    features = jnp.where(first_core, features_first, features_second)
    next_part = feat_reduce_scatter(decode(features, next_full), None, feat_index, n_feat)
    outgoing_now = next_part.astype(jnp.bfloat16)
    incoming = lax.ppermute(outgoing_now, "layer", [(0, 1)])
    recon_second = own_second + incoming.astype(jnp.float32)

    recon_out = jnp.where(first_core, recon_first, recon_second).astype(jnp.bfloat16)
    return (recon_out[None], outgoing_now[None])


def solution(mesh):
    devices = mesh.devices
    n_y = len({device.coords[1] for device in devices.reshape(-1)})
    split_mesh = Mesh(
        devices.reshape(devices.shape[:2] + (devices.shape[2] // n_y, n_y)),
        ("layer", "feat", "tz", "ty"),
    )
    return jax.shard_map(
        shards,
        mesh=split_mesh,
        in_specs=(
            P(TOK, "feat"),
            P("layer", TOK, "feat"),
            P(TOK, "feat"),
            P("layer", None, "feat"),
            P("layer", "feat"),
            P("layer", "feat", TOK),
            P("layer", "feat", TOK),
            P("layer", TOK, None),
            P("layer", TOK),
        ),
        out_specs=(P("layer", TOK, "feat"), P("layer", TOK, "feat")),
        check_vma=False,
    )
```

```python
import jax
import jax.numpy as jnp
from jax import lax
from jax.sharding import Mesh, PartitionSpec as P

BLOCK = 128
TILE = 128
GROUP = ("layer", "feat")
TOK = ("tz", "ty")


def within_layer(shard, section, shift, n_feat):
    if section is None:
        return lax.ppermute(shard, "feat", [(i, (i + shift) % n_feat) for i in range(n_feat)])
    pairs = [
        (section * n_feat + i, section * n_feat + (i + shift) % n_feat) for i in range(n_feat)
    ]
    return lax.ppermute(shard, GROUP, pairs)


def feat_gather(part, section, feat_index, n_feat):
    received = [part] + [within_layer(part, section, k, n_feat) for k in range(1, n_feat)]
    blocks = []
    for j in range(n_feat):
        block = jnp.zeros_like(part)
        for k in range(n_feat):
            block = jnp.where((feat_index - k) % n_feat == j, received[k], block)
        blocks.append(block)
    return jnp.concatenate(blocks, axis=-1)


def feat_reduce_scatter(terms, section, feat_index, n_feat):
    cols = terms.shape[-1] // n_feat
    total = lax.dynamic_slice_in_dim(terms, feat_index * cols, cols, terms.ndim - 1).astype(
        jnp.float32
    )
    for k in range(1, n_feat):
        target = (feat_index + k) % n_feat
        piece = lax.dynamic_slice_in_dim(terms, target * cols, cols, terms.ndim - 1)
        total = total + within_layer(piece, section, k, n_feat).astype(jnp.float32)
    return total


def feature_mask(block_list, block_count, feat_index, blocks_dev):
    listed = block_list[0]
    in_use = jnp.arange(listed.shape[1], dtype=jnp.int32)[None, :] < block_count[0][:, None]
    own_blocks = feat_index * blocks_dev + jnp.arange(blocks_dev, dtype=jnp.int32)
    matches = (listed[:, None, :] == own_blocks[None, :, None]) & in_use[:, None, :]
    active = jnp.any(matches, axis=2).astype(jnp.float32)
    return jnp.repeat(jnp.repeat(active, TILE, axis=0), BLOCK, axis=1)


def encode(gathered, enc_weight, enc_bias, mask):
    preact = (
        jnp.dot(gathered, enc_weight[0], preferred_element_type=jnp.float32) + enc_bias[0][None, :]
    )
    return (jax.nn.relu(preact) * mask).astype(jnp.bfloat16)


def decode(features, full):
    return jnp.dot(features, full, preferred_element_type=jnp.float32).astype(jnp.bfloat16)


def shards(
    resid_in, attn_out, carry_in, enc_weight, enc_bias, dec_own, dec_next, block_list, block_count
):
    n_feat = lax.axis_size("feat")
    section_index = lax.axis_index("layer")
    feat_index = lax.axis_index("feat")
    blocks_dev = enc_weight.shape[2] // BLOCK
    first_core = section_index == 0
    own_full = lax.all_gather(dec_own[0], TOK, axis=1, tiled=True)
    next_full = lax.all_gather(dec_next[0], TOK, axis=1, tiled=True)
    mask = feature_mask(block_list, block_count, feat_index, blocks_dev)
    attention = attn_out[0].astype(jnp.float32)

    def encoded(source, section):
        return lax.cond(
            section_index == section,
            lambda inner: encode(inner, enc_weight, enc_bias, mask),
            lambda inner: jnp.zeros((inner.shape[0], enc_weight.shape[2]), jnp.bfloat16),
            source,
        )

    features_first = encoded(feat_gather(resid_in, 0, feat_index, n_feat), 0)
    own_first = feat_reduce_scatter(decode(features_first, own_full), 0, feat_index, n_feat)
    recon_first = own_first + carry_in.astype(jnp.float32)
    residual_next = (resid_in.astype(jnp.float32) + attention + recon_first).astype(jnp.bfloat16)
    residual_next = lax.ppermute(residual_next, "layer", [(0, 1)])

    features_second = encoded(feat_gather(residual_next, 1, feat_index, n_feat), 1)
    own_second = feat_reduce_scatter(decode(features_second, own_full), 1, feat_index, n_feat)

    features = jnp.where(first_core, features_first, features_second)
    next_part = feat_reduce_scatter(decode(features, next_full), None, feat_index, n_feat)
    outgoing_now = next_part.astype(jnp.bfloat16)
    incoming = lax.ppermute(outgoing_now, "layer", [(0, 1)])
    recon_second = own_second + incoming.astype(jnp.float32)

    recon_out = jnp.where(first_core, recon_first, recon_second).astype(jnp.bfloat16)
    return (recon_out[None], outgoing_now[None])


def solution(mesh):
    devices = mesh.devices
    n_y = len({device.coords[1] for device in devices.reshape(-1)})
    split_mesh = Mesh(
        devices.reshape(devices.shape[:2] + (devices.shape[2] // n_y, n_y)),
        ("layer", "feat", "tz", "ty"),
    )
    return jax.shard_map(
        shards,
        mesh=split_mesh,
        in_specs=(
            P(TOK, "feat"),
            P("layer", TOK, "feat"),
            P(TOK, "feat"),
            P("layer", None, "feat"),
            P("layer", "feat"),
            P("layer", "feat", TOK),
            P("layer", "feat", TOK),
            P("layer", TOK, None),
            P("layer", TOK),
        ),
        out_specs=(P("layer", TOK, "feat"), P("layer", TOK, "feat")),
        check_vma=False,
    )
```

```python
import jax
import jax.numpy as jnp
from jax import lax
from jax.sharding import PartitionSpec as P

BLOCK = 128
TILE = 128
GROUP = ("layer", "feat")


def within_layer(shard, section, shift, n_feat):
    if section is None:
        return lax.ppermute(shard, "feat", [(i, (i + shift) % n_feat) for i in range(n_feat)])
    pairs = [
        (section * n_feat + i, section * n_feat + (i + shift) % n_feat) for i in range(n_feat)
    ]
    return lax.ppermute(shard, GROUP, pairs)


def feat_gather(part, section, feat_index, n_feat):
    received = [part] + [within_layer(part, section, k, n_feat) for k in range(1, n_feat)]
    blocks = []
    for j in range(n_feat):
        block = jnp.zeros_like(part)
        for k in range(n_feat):
            block = jnp.where((feat_index - k) % n_feat == j, received[k], block)
        blocks.append(block)
    return jnp.concatenate(blocks, axis=-1)


def feat_reduce_scatter(terms, section, feat_index, n_feat):
    cols = terms.shape[-1] // n_feat
    total = lax.dynamic_slice_in_dim(terms, feat_index * cols, cols, terms.ndim - 1).astype(
        jnp.float32
    )
    for k in range(1, n_feat):
        target = (feat_index + k) % n_feat
        piece = lax.dynamic_slice_in_dim(terms, target * cols, cols, terms.ndim - 1)
        total = total + within_layer(piece, section, k, n_feat).astype(jnp.float32)
    return total


def decode_scatter(features, decoder, feat_index, n_feat):
    cols = decoder.shape[1] // n_feat
    total = None
    for k in sorted(range(n_feat), key=lambda shift: (-min(shift, n_feat - shift), shift)):
        target = (feat_index + k) % n_feat
        chunk = lax.dynamic_slice_in_dim(decoder, target * cols, cols, 1)
        piece = jnp.dot(features, chunk, preferred_element_type=jnp.float32).astype(jnp.bfloat16)
        if k:
            piece = within_layer(piece, None, k, n_feat)
        piece = piece.astype(jnp.float32)
        total = piece if total is None else total + piece
    return total


def feature_mask(block_list, block_count, feat_index, blocks_dev):
    listed = block_list[0]
    in_use = jnp.arange(listed.shape[1], dtype=jnp.int32)[None, :] < block_count[0][:, None]
    own_blocks = feat_index * blocks_dev + jnp.arange(blocks_dev, dtype=jnp.int32)
    matches = (listed[:, None, :] == own_blocks[None, :, None]) & in_use[:, None, :]
    active = jnp.any(matches, axis=2).astype(jnp.float32)
    return jnp.repeat(jnp.repeat(active, TILE, axis=0), BLOCK, axis=1)


def encode(gathered, enc_weight, enc_bias, mask):
    preact = (
        jnp.dot(gathered, enc_weight[0], preferred_element_type=jnp.float32) + enc_bias[0][None, :]
    )
    return (jax.nn.relu(preact) * mask).astype(jnp.bfloat16)


def shards(
    resid_in, attn_out, carry_in, enc_weight, enc_bias, dec_own, dec_next, block_list, block_count
):
    n_feat = lax.axis_size("feat")
    section_index = lax.axis_index("layer")
    feat_index = lax.axis_index("feat")
    blocks_dev = enc_weight.shape[2] // BLOCK
    first_core = section_index == 0
    swapped_next = lax.ppermute(dec_next[0], "layer", [(0, 1), (1, 0)])
    first_dec = jnp.where(first_core, dec_own[0], swapped_next)
    second_dec = jnp.where(first_core, swapped_next, dec_own[0])
    first_full = lax.all_gather(first_dec, "tok", axis=1, tiled=True)
    second_full = lax.all_gather(second_dec, "tok", axis=1, tiled=True)
    mask = feature_mask(block_list, block_count, feat_index, blocks_dev)
    attention = attn_out[0].astype(jnp.float32)

    gathered = feat_gather(resid_in, 0, feat_index, n_feat)
    features = lax.cond(
        first_core,
        lambda source: encode(source, enc_weight, enc_bias, mask),
        lambda source: jnp.zeros((source.shape[0], enc_weight.shape[2]), jnp.bfloat16),
        gathered,
    )
    features = jnp.where(first_core, features, lax.ppermute(features, "layer", [(0, 1)]))
    summed = decode_scatter(features, first_full, feat_index, n_feat)
    recon_first = summed + carry_in.astype(jnp.float32)
    residual_next = (resid_in.astype(jnp.float32) + attention + recon_first).astype(jnp.bfloat16)
    outgoing_first = summed.astype(jnp.bfloat16)
    swapped = lax.ppermute(
        jnp.where(first_core, residual_next, outgoing_first), "layer", [(0, 1), (1, 0)]
    )

    gathered = feat_gather(swapped, 1, feat_index, n_feat)
    features = lax.cond(
        first_core,
        lambda source: jnp.zeros((source.shape[0], enc_weight.shape[2]), jnp.bfloat16),
        lambda source: encode(source, enc_weight, enc_bias, mask),
        gathered,
    )
    features = jnp.where(first_core, lax.ppermute(features, "layer", [(1, 0)]), features)
    summed = decode_scatter(features, second_full, feat_index, n_feat)
    recon_second = summed + outgoing_first.astype(jnp.float32)
    outgoing_second = lax.ppermute(summed.astype(jnp.bfloat16), "layer", [(0, 1)])

    recon_out = jnp.where(first_core, recon_first, recon_second).astype(jnp.bfloat16)
    outgoing_out = jnp.where(first_core, swapped, outgoing_second)
    return (recon_out[None], outgoing_out[None])


def solution(mesh):
    return jax.shard_map(
        shards,
        mesh=mesh,
        in_specs=(
            P("tok", "feat"),
            P("layer", "tok", "feat"),
            P("tok", "feat"),
            P("layer", None, "feat"),
            P("layer", "feat"),
            P("layer", "feat", "tok"),
            P("layer", "feat", "tok"),
            P("layer", "tok", None),
            P("layer", "tok"),
        ),
        out_specs=(P("layer", "tok", "feat"), P("layer", "tok", "feat")),
        check_vma=False,
    )
```

```python
import jax
import jax.numpy as jnp
from jax import lax
from jax.sharding import PartitionSpec as P

BLOCK = 128
TILE = 128
GROUP = ("layer", "feat")


def within_layer(shard, section, shift, n_feat):
    if section is None:
        return lax.ppermute(shard, "feat", [(i, (i + shift) % n_feat) for i in range(n_feat)])
    pairs = [
        (section * n_feat + i, section * n_feat + (i + shift) % n_feat) for i in range(n_feat)
    ]
    return lax.ppermute(shard, GROUP, pairs)


def feat_gather(part, section, feat_index, n_feat):
    received = [part] + [within_layer(part, section, k, n_feat) for k in range(1, n_feat)]
    blocks = []
    for j in range(n_feat):
        block = jnp.zeros_like(part)
        for k in range(n_feat):
            block = jnp.where((feat_index - k) % n_feat == j, received[k], block)
        blocks.append(block)
    return jnp.concatenate(blocks, axis=-1)


def feat_reduce_scatter(terms, section, feat_index, n_feat):
    cols = terms.shape[-1] // n_feat
    total = lax.dynamic_slice_in_dim(terms, feat_index * cols, cols, terms.ndim - 1).astype(
        jnp.float32
    )
    for k in range(1, n_feat):
        target = (feat_index + k) % n_feat
        piece = lax.dynamic_slice_in_dim(terms, target * cols, cols, terms.ndim - 1)
        total = total + within_layer(piece, section, k, n_feat).astype(jnp.float32)
    return total


def decode_scatter(features, decoder, feat_index, n_feat):
    part = jnp.dot(features, decoder, preferred_element_type=jnp.float32).astype(jnp.bfloat16)
    rows, columns = part.shape
    chunks = part.reshape(rows, n_feat, columns // n_feat).transpose(1, 0, 2)
    received = lax.all_to_all(chunks, "feat", 0, 0, tiled=True)
    return jnp.sum(received.astype(jnp.float32), axis=0)


def feature_mask(block_list, block_count, feat_index, blocks_dev):
    listed = block_list[0]
    in_use = jnp.arange(listed.shape[1], dtype=jnp.int32)[None, :] < block_count[0][:, None]
    own_blocks = feat_index * blocks_dev + jnp.arange(blocks_dev, dtype=jnp.int32)
    matches = (listed[:, None, :] == own_blocks[None, :, None]) & in_use[:, None, :]
    active = jnp.any(matches, axis=2).astype(jnp.float32)
    return jnp.repeat(jnp.repeat(active, TILE, axis=0), BLOCK, axis=1)


def encode(gathered, enc_weight, enc_bias, mask):
    preact = (
        jnp.dot(gathered, enc_weight[0], preferred_element_type=jnp.float32) + enc_bias[0][None, :]
    )
    return (jax.nn.relu(preact) * mask).astype(jnp.bfloat16)


def shards(
    resid_in, attn_out, carry_in, enc_weight, enc_bias, dec_own, dec_next, block_list, block_count
):
    n_feat = lax.axis_size("feat")
    section_index = lax.axis_index("layer")
    feat_index = lax.axis_index("feat")
    blocks_dev = enc_weight.shape[2] // BLOCK
    first_core = section_index == 0
    swapped_next = lax.ppermute(dec_next[0], "layer", [(0, 1), (1, 0)])
    first_dec = jnp.where(first_core, dec_own[0], swapped_next)
    second_dec = jnp.where(first_core, swapped_next, dec_own[0])
    first_full = lax.all_gather(first_dec, "tok", axis=1, tiled=True)
    second_full = lax.all_gather(second_dec, "tok", axis=1, tiled=True)
    mask = feature_mask(block_list, block_count, feat_index, blocks_dev)
    attention = attn_out[0].astype(jnp.float32)

    gathered = feat_gather(resid_in, 0, feat_index, n_feat)
    features = lax.cond(
        first_core,
        lambda source: encode(source, enc_weight, enc_bias, mask),
        lambda source: jnp.zeros((source.shape[0], enc_weight.shape[2]), jnp.bfloat16),
        gathered,
    )
    features = jnp.where(first_core, features, lax.ppermute(features, "layer", [(0, 1)]))
    summed = decode_scatter(features, first_full, feat_index, n_feat)
    recon_first = summed + carry_in.astype(jnp.float32)
    residual_next = (resid_in.astype(jnp.float32) + attention + recon_first).astype(jnp.bfloat16)
    outgoing_first = summed.astype(jnp.bfloat16)
    swapped = lax.ppermute(
        jnp.where(first_core, residual_next, outgoing_first), "layer", [(0, 1), (1, 0)]
    )

    gathered = feat_gather(swapped, 1, feat_index, n_feat)
    features = lax.cond(
        first_core,
        lambda source: jnp.zeros((source.shape[0], enc_weight.shape[2]), jnp.bfloat16),
        lambda source: encode(source, enc_weight, enc_bias, mask),
        gathered,
    )
    features = jnp.where(first_core, lax.ppermute(features, "layer", [(1, 0)]), features)
    summed = decode_scatter(features, second_full, feat_index, n_feat)
    recon_second = summed + outgoing_first.astype(jnp.float32)
    outgoing_second = lax.ppermute(summed.astype(jnp.bfloat16), "layer", [(0, 1)])

    recon_out = jnp.where(first_core, recon_first, recon_second).astype(jnp.bfloat16)
    outgoing_out = jnp.where(first_core, swapped, outgoing_second)
    return (recon_out[None], outgoing_out[None])


def solution(mesh):
    return jax.shard_map(
        shards,
        mesh=mesh,
        in_specs=(
            P("tok", "feat"),
            P("layer", "tok", "feat"),
            P("tok", "feat"),
            P("layer", None, "feat"),
            P("layer", "feat"),
            P("layer", "feat", "tok"),
            P("layer", "feat", "tok"),
            P("layer", "tok", None),
            P("layer", "tok"),
        ),
        out_specs=(P("layer", "tok", "feat"), P("layer", "tok", "feat")),
        check_vma=False,
    )
```

```python
import jax
import jax.numpy as jnp
from jax import lax
from jax.sharding import PartitionSpec as P

BLOCK = 128
TILE = 128
GROUP = ("layer", "feat")


def within_layer(shard, section, shift, n_feat):
    if section is None:
        return lax.ppermute(shard, "feat", [(i, (i + shift) % n_feat) for i in range(n_feat)])
    pairs = [
        (section * n_feat + i, section * n_feat + (i + shift) % n_feat) for i in range(n_feat)
    ]
    return lax.ppermute(shard, GROUP, pairs)


def feat_gather(part, section, feat_index, n_feat):
    received = [part] + [within_layer(part, section, k, n_feat) for k in range(1, n_feat)]
    blocks = []
    for j in range(n_feat):
        block = jnp.zeros_like(part)
        for k in range(n_feat):
            block = jnp.where((feat_index - k) % n_feat == j, received[k], block)
        blocks.append(block)
    return jnp.concatenate(blocks, axis=-1)


def feat_reduce_scatter(terms, section, feat_index, n_feat):
    cols = terms.shape[-1] // n_feat
    total = lax.dynamic_slice_in_dim(terms, feat_index * cols, cols, terms.ndim - 1).astype(
        jnp.float32
    )
    for k in range(1, n_feat):
        target = (feat_index + k) % n_feat
        piece = lax.dynamic_slice_in_dim(terms, target * cols, cols, terms.ndim - 1)
        total = total + within_layer(piece, section, k, n_feat).astype(jnp.float32)
    return total


def decode_scatter(features, decoder, feat_index, n_feat):
    cols = decoder.shape[1] // n_feat
    total = None
    for k in sorted(range(n_feat), key=lambda shift: (-min(shift, n_feat - shift), shift)):
        target = (feat_index + k) % n_feat
        chunk = lax.dynamic_slice_in_dim(decoder, target * cols, cols, 1)
        piece = jnp.dot(features, chunk, preferred_element_type=jnp.float32).astype(jnp.bfloat16)
        if k:
            piece = within_layer(piece, None, k, n_feat)
        else:
            piece = lax.optimization_barrier(piece)
        piece = piece.astype(jnp.float32)
        total = piece if total is None else total + piece
    return total


def feature_mask(block_list, block_count, feat_index, blocks_dev):
    listed = block_list[0]
    in_use = jnp.arange(listed.shape[1], dtype=jnp.int32)[None, :] < block_count[0][:, None]
    own_blocks = feat_index * blocks_dev + jnp.arange(blocks_dev, dtype=jnp.int32)
    matches = (listed[:, None, :] == own_blocks[None, :, None]) & in_use[:, None, :]
    active = jnp.any(matches, axis=2).astype(jnp.float32)
    return jnp.repeat(jnp.repeat(active, TILE, axis=0), BLOCK, axis=1)


def encode(gathered, enc_weight, enc_bias, mask):
    preact = (
        jnp.dot(gathered, enc_weight[0], preferred_element_type=jnp.float32) + enc_bias[0][None, :]
    )
    return (jax.nn.relu(preact) * mask).astype(jnp.bfloat16)


def shards(
    resid_in, attn_out, carry_in, enc_weight, enc_bias, dec_own, dec_next, block_list, block_count
):
    n_feat = lax.axis_size("feat")
    section_index = lax.axis_index("layer")
    feat_index = lax.axis_index("feat")
    blocks_dev = enc_weight.shape[2] // BLOCK
    first_core = section_index == 0
    swapped_next = lax.ppermute(dec_next[0], "layer", [(0, 1), (1, 0)])
    first_dec = jnp.where(first_core, dec_own[0], swapped_next)
    second_dec = jnp.where(first_core, swapped_next, dec_own[0])
    first_full = lax.all_gather(first_dec, "tok", axis=1, tiled=True)
    second_full = lax.all_gather(second_dec, "tok", axis=1, tiled=True)
    mask = feature_mask(block_list, block_count, feat_index, blocks_dev)
    attention = attn_out[0].astype(jnp.float32)

    gathered = feat_gather(resid_in, 0, feat_index, n_feat)
    features = lax.cond(
        first_core,
        lambda source: encode(source, enc_weight, enc_bias, mask),
        lambda source: jnp.zeros((source.shape[0], enc_weight.shape[2]), jnp.bfloat16),
        gathered,
    )
    features = jnp.where(first_core, features, lax.ppermute(features, "layer", [(0, 1)]))
    summed = decode_scatter(features, first_full, feat_index, n_feat)
    recon_first = summed + carry_in.astype(jnp.float32)
    residual_next = (resid_in.astype(jnp.float32) + attention + recon_first).astype(jnp.bfloat16)
    outgoing_first = summed.astype(jnp.bfloat16)
    swapped = lax.ppermute(
        jnp.where(first_core, residual_next, outgoing_first), "layer", [(0, 1), (1, 0)]
    )

    gathered = feat_gather(swapped, 1, feat_index, n_feat)
    features = lax.cond(
        first_core,
        lambda source: jnp.zeros((source.shape[0], enc_weight.shape[2]), jnp.bfloat16),
        lambda source: encode(source, enc_weight, enc_bias, mask),
        gathered,
    )
    features = jnp.where(first_core, lax.ppermute(features, "layer", [(1, 0)]), features)
    summed = decode_scatter(features, second_full, feat_index, n_feat)
    recon_second = summed + outgoing_first.astype(jnp.float32)
    outgoing_second = lax.ppermute(summed.astype(jnp.bfloat16), "layer", [(0, 1)])

    recon_out = jnp.where(first_core, recon_first, recon_second).astype(jnp.bfloat16)
    outgoing_out = jnp.where(first_core, swapped, outgoing_second)
    return (recon_out[None], outgoing_out[None])


def solution(mesh):
    return jax.shard_map(
        shards,
        mesh=mesh,
        in_specs=(
            P("tok", "feat"),
            P("layer", "tok", "feat"),
            P("tok", "feat"),
            P("layer", None, "feat"),
            P("layer", "feat"),
            P("layer", "feat", "tok"),
            P("layer", "feat", "tok"),
            P("layer", "tok", None),
            P("layer", "tok"),
        ),
        out_specs=(P("layer", "tok", "feat"), P("layer", "tok", "feat")),
        check_vma=False,
    )
```

```python
import jax
import jax.numpy as jnp
from jax import lax
from jax.sharding import PartitionSpec as P

BLOCK = 128
TILE = 128
GROUP = ("layer", "feat")


def within_layer(shard, section, shift, n_feat):
    if section is None:
        return lax.ppermute(shard, "feat", [(i, (i + shift) % n_feat) for i in range(n_feat)])
    pairs = [
        (section * n_feat + i, section * n_feat + (i + shift) % n_feat) for i in range(n_feat)
    ]
    return lax.ppermute(shard, GROUP, pairs)


def feat_gather(part, section, feat_index, n_feat):
    received = [part] + [within_layer(part, section, k, n_feat) for k in range(1, n_feat)]
    blocks = []
    for j in range(n_feat):
        block = jnp.zeros_like(part)
        for k in range(n_feat):
            block = jnp.where((feat_index - k) % n_feat == j, received[k], block)
        blocks.append(block)
    return jnp.concatenate(blocks, axis=-1)


def feat_reduce_scatter(terms, section, feat_index, n_feat):
    cols = terms.shape[-1] // n_feat
    total = lax.dynamic_slice_in_dim(terms, feat_index * cols, cols, terms.ndim - 1).astype(
        jnp.float32
    )
    for k in range(1, n_feat):
        target = (feat_index + k) % n_feat
        piece = lax.dynamic_slice_in_dim(terms, target * cols, cols, terms.ndim - 1)
        total = total + within_layer(piece, section, k, n_feat).astype(jnp.float32)
    return total


def decode_scatter(features, decoder, feat_index, n_feat):
    decoder = decoder if isinstance(decoder, tuple) else (decoder,)
    cols = decoder[0].shape[1] // n_feat
    total = None
    for k in sorted(range(n_feat), key=lambda shift: (-min(shift, n_feat - shift), shift)):
        target = (feat_index + k) % n_feat
        piece = None
        row = 0
        for part in decoder:
            chunk = lax.dynamic_slice_in_dim(part, target * cols, cols, 1)
            product = jnp.dot(
                features[:, row : row + part.shape[0]], chunk, preferred_element_type=jnp.float32
            )
            piece = product if piece is None else piece + product
            row += part.shape[0]
        piece = piece.astype(jnp.bfloat16)
        if k:
            piece = within_layer(piece, None, k, n_feat)
        else:
            piece = lax.optimization_barrier(piece)
        piece = piece.astype(jnp.float32)
        total = piece if total is None else total + piece
    return total


def feature_mask(block_list, block_count, feat_index, blocks_dev):
    listed = block_list[0]
    in_use = jnp.arange(listed.shape[1], dtype=jnp.int32)[None, :] < block_count[0][:, None]
    own_blocks = feat_index * blocks_dev + jnp.arange(blocks_dev, dtype=jnp.int32)
    matches = (listed[:, None, :] == own_blocks[None, :, None]) & in_use[:, None, :]
    active = jnp.any(matches, axis=2).astype(jnp.float32)
    return jnp.repeat(jnp.repeat(active, TILE, axis=0), BLOCK, axis=1)


def encode(gathered, enc_weight, enc_bias, mask):
    preact = (
        jnp.dot(gathered, enc_weight[0], preferred_element_type=jnp.float32) + enc_bias[0][None, :]
    )
    return (jax.nn.relu(preact) * mask).astype(jnp.bfloat16)


def shards(
    resid_in, attn_out, carry_in, enc_weight, enc_bias, dec_own, dec_next, block_list, block_count
):
    n_feat = lax.axis_size("feat")
    section_index = lax.axis_index("layer")
    feat_index = lax.axis_index("feat")
    blocks_dev = enc_weight.shape[2] // BLOCK
    first_core = section_index == 0
    swapped_next = lax.ppermute(dec_next[0], "layer", [(0, 1), (1, 0)])
    first_dec = jnp.where(first_core, dec_own[0], swapped_next)
    second_dec = jnp.where(first_core, swapped_next, dec_own[0])
    half = second_dec.shape[0] // 2
    early = lax.all_gather(
        jnp.concatenate([first_dec, second_dec[:half]]), "tok", axis=1, tiled=True
    )
    first_full = early[: first_dec.shape[0]]
    second_full = (early[first_dec.shape[0] :], lax.all_gather(second_dec[half:], "tok", axis=1, tiled=True))
    mask = feature_mask(block_list, block_count, feat_index, blocks_dev)
    attention = attn_out[0].astype(jnp.float32)

    gathered = feat_gather(resid_in, 0, feat_index, n_feat)
    features = lax.cond(
        first_core,
        lambda source: encode(source, enc_weight, enc_bias, mask),
        lambda source: jnp.zeros((source.shape[0], enc_weight.shape[2]), jnp.bfloat16),
        gathered,
    )
    features = jnp.where(first_core, features, lax.ppermute(features, "layer", [(0, 1)]))
    summed = decode_scatter(features, first_full, feat_index, n_feat)
    recon_first = summed + carry_in.astype(jnp.float32)
    residual_next = (resid_in.astype(jnp.float32) + attention + recon_first).astype(jnp.bfloat16)
    outgoing_first = summed.astype(jnp.bfloat16)
    swapped = lax.ppermute(
        jnp.where(first_core, residual_next, outgoing_first), "layer", [(0, 1), (1, 0)]
    )

    gathered = feat_gather(swapped, 1, feat_index, n_feat)
    features = lax.cond(
        first_core,
        lambda source: jnp.zeros((source.shape[0], enc_weight.shape[2]), jnp.bfloat16),
        lambda source: encode(source, enc_weight, enc_bias, mask),
        gathered,
    )
    features = jnp.where(first_core, lax.ppermute(features, "layer", [(1, 0)]), features)
    summed = decode_scatter(features, second_full, feat_index, n_feat)
    recon_second = summed + outgoing_first.astype(jnp.float32)
    outgoing_second = lax.ppermute(summed.astype(jnp.bfloat16), "layer", [(0, 1)])

    recon_out = jnp.where(first_core, recon_first, recon_second).astype(jnp.bfloat16)
    outgoing_out = jnp.where(first_core, swapped, outgoing_second)
    return (recon_out[None], outgoing_out[None])


def solution(mesh):
    return jax.shard_map(
        shards,
        mesh=mesh,
        in_specs=(
            P("tok", "feat"),
            P("layer", "tok", "feat"),
            P("tok", "feat"),
            P("layer", None, "feat"),
            P("layer", "feat"),
            P("layer", "feat", "tok"),
            P("layer", "feat", "tok"),
            P("layer", "tok", None),
            P("layer", "tok"),
        ),
        out_specs=(P("layer", "tok", "feat"), P("layer", "tok", "feat")),
        check_vma=False,
    )
```

```python
import jax
import jax.numpy as jnp
from jax import lax
from jax.sharding import PartitionSpec as P

BLOCK = 128
TILE = 128
GROUP = ("layer", "feat")


def within_layer(shard, section, shift, n_feat):
    if section is None:
        return lax.ppermute(shard, "feat", [(i, (i + shift) % n_feat) for i in range(n_feat)])
    pairs = [
        (section * n_feat + i, section * n_feat + (i + shift) % n_feat) for i in range(n_feat)
    ]
    return lax.ppermute(shard, GROUP, pairs)


def feat_gather(part, section, feat_index, n_feat):
    received = [part] + [within_layer(part, section, k, n_feat) for k in range(1, n_feat)]
    blocks = []
    for j in range(n_feat):
        block = jnp.zeros_like(part)
        for k in range(n_feat):
            block = jnp.where((feat_index - k) % n_feat == j, received[k], block)
        blocks.append(block)
    return jnp.concatenate(blocks, axis=-1)


def feat_reduce_scatter(terms, section, feat_index, n_feat):
    cols = terms.shape[-1] // n_feat
    total = lax.dynamic_slice_in_dim(terms, feat_index * cols, cols, terms.ndim - 1).astype(
        jnp.float32
    )
    for k in range(1, n_feat):
        target = (feat_index + k) % n_feat
        piece = lax.dynamic_slice_in_dim(terms, target * cols, cols, terms.ndim - 1)
        total = total + within_layer(piece, section, k, n_feat).astype(jnp.float32)
    return total


def decode_scatter(features, decoder, feat_index, n_feat):
    cols = decoder.shape[1] // n_feat
    total = None
    for k in sorted(range(n_feat), key=lambda shift: (-min(shift, n_feat - shift), shift)):
        target = (feat_index + k) % n_feat
        chunk = lax.dynamic_slice_in_dim(decoder, target * cols, cols, 1)
        piece = jnp.dot(features, chunk, preferred_element_type=jnp.float32).astype(jnp.bfloat16)
        if k:
            piece = within_layer(piece, None, k, n_feat)
        else:
            piece = lax.optimization_barrier(piece)
        piece = piece.astype(jnp.float32)
        total = piece if total is None else total + piece
    return total


def decode_scatter_across(features, decoder, feat_index, n_feat):
    cols = decoder.shape[1] // n_feat
    own_total = None
    next_total = None
    for k in sorted(range(n_feat), key=lambda shift: (-min(shift, n_feat - shift), shift)):
        target = (feat_index + k) % n_feat
        chunk = lax.dynamic_slice_in_dim(decoder, target * cols, cols, 1)
        piece = jnp.dot(features, chunk, preferred_element_type=jnp.float32).astype(jnp.bfloat16)
        cross = lax.ppermute(
            piece, GROUP, [(i, n_feat + (i + k) % n_feat) for i in range(n_feat)]
        ).astype(jnp.float32)
        next_total = cross if next_total is None else next_total + cross
        if k:
            mine = within_layer(piece, 1, k, n_feat)
        else:
            mine = lax.optimization_barrier(piece)
        mine = mine.astype(jnp.float32)
        own_total = mine if own_total is None else own_total + mine
    return own_total, next_total


def feature_mask(block_list, block_count, feat_index, blocks_dev):
    listed = block_list[0]
    in_use = jnp.arange(listed.shape[1], dtype=jnp.int32)[None, :] < block_count[0][:, None]
    own_blocks = feat_index * blocks_dev + jnp.arange(blocks_dev, dtype=jnp.int32)
    matches = (listed[:, None, :] == own_blocks[None, :, None]) & in_use[:, None, :]
    active = jnp.any(matches, axis=2).astype(jnp.float32)
    return jnp.repeat(jnp.repeat(active, TILE, axis=0), BLOCK, axis=1)


def encode(gathered, enc_weight, enc_bias, mask):
    preact = (
        jnp.dot(gathered, enc_weight[0], preferred_element_type=jnp.float32) + enc_bias[0][None, :]
    )
    return (jax.nn.relu(preact) * mask).astype(jnp.bfloat16)


def shards(
    resid_in, attn_out, carry_in, enc_weight, enc_bias, dec_own, dec_next, block_list, block_count
):
    n_feat = lax.axis_size("feat")
    section_index = lax.axis_index("layer")
    feat_index = lax.axis_index("feat")
    blocks_dev = enc_weight.shape[2] // BLOCK
    first_core = section_index == 0
    swapped_next = lax.ppermute(dec_next[0], "layer", [(0, 1), (1, 0)])
    first_dec = jnp.where(first_core, dec_own[0], swapped_next)
    second_dec = jnp.where(first_core, swapped_next, dec_own[0])
    first_full = lax.all_gather(first_dec, "tok", axis=1, tiled=True)
    second_full = lax.all_gather(second_dec, "tok", axis=1, tiled=True)
    mask = feature_mask(block_list, block_count, feat_index, blocks_dev)
    attention = attn_out[0].astype(jnp.float32)

    gathered = feat_gather(resid_in, 0, feat_index, n_feat)
    features = lax.cond(
        first_core,
        lambda source: encode(source, enc_weight, enc_bias, mask),
        lambda source: jnp.zeros((source.shape[0], enc_weight.shape[2]), jnp.bfloat16),
        gathered,
    )
    features = jnp.where(first_core, features, lax.ppermute(features, "layer", [(0, 1)]))
    summed = decode_scatter(features, first_full, feat_index, n_feat)
    recon_first = summed + carry_in.astype(jnp.float32)
    residual_next = (resid_in.astype(jnp.float32) + attention + recon_first).astype(jnp.bfloat16)
    outgoing_first = summed.astype(jnp.bfloat16)
    swapped = lax.ppermute(
        jnp.where(first_core, residual_next, outgoing_first), "layer", [(0, 1), (1, 0)]
    )

    gathered = feat_gather(swapped, 1, feat_index, n_feat)
    features = lax.cond(
        first_core,
        lambda source: jnp.zeros((source.shape[0], enc_weight.shape[2]), jnp.bfloat16),
        lambda source: encode(source, enc_weight, enc_bias, mask),
        gathered,
    )
    features = jnp.where(first_core, lax.ppermute(features, "layer", [(1, 0)]), features)
    summed, next_second = decode_scatter_across(features, second_full, feat_index, n_feat)
    recon_second = summed + outgoing_first.astype(jnp.float32)
    outgoing_second = next_second.astype(jnp.bfloat16)

    recon_out = jnp.where(first_core, recon_first, recon_second).astype(jnp.bfloat16)
    outgoing_out = jnp.where(first_core, swapped, outgoing_second)
    return (recon_out[None], outgoing_out[None])


def solution(mesh):
    return jax.shard_map(
        shards,
        mesh=mesh,
        in_specs=(
            P("tok", "feat"),
            P("layer", "tok", "feat"),
            P("tok", "feat"),
            P("layer", None, "feat"),
            P("layer", "feat"),
            P("layer", "feat", "tok"),
            P("layer", "feat", "tok"),
            P("layer", "tok", None),
            P("layer", "tok"),
        ),
        out_specs=(P("layer", "tok", "feat"), P("layer", "tok", "feat")),
        check_vma=False,
    )
```

```python
import jax
import jax.numpy as jnp
from jax import lax
from jax.sharding import Mesh, PartitionSpec as P

BLOCK = 128
TILE = 128
GROUP = ("layer", "feat")
TOK = ("tz", "ty")


def within_layer(shard, section, shift, n_feat):
    if section is None:
        return lax.ppermute(shard, "feat", [(i, (i + shift) % n_feat) for i in range(n_feat)])
    pairs = [
        (section * n_feat + i, section * n_feat + (i + shift) % n_feat) for i in range(n_feat)
    ]
    return lax.ppermute(shard, GROUP, pairs)


def feat_gather(part, section, feat_index, n_feat):
    received = [part] + [within_layer(part, section, k, n_feat) for k in range(1, n_feat)]
    blocks = []
    for j in range(n_feat):
        block = jnp.zeros_like(part)
        for k in range(n_feat):
            block = jnp.where((feat_index - k) % n_feat == j, received[k], block)
        blocks.append(block)
    return jnp.concatenate(blocks, axis=-1)


def feat_reduce_scatter(terms, section, feat_index, n_feat):
    cols = terms.shape[-1] // n_feat
    total = lax.dynamic_slice_in_dim(terms, feat_index * cols, cols, terms.ndim - 1).astype(
        jnp.float32
    )
    for k in range(1, n_feat):
        target = (feat_index + k) % n_feat
        piece = lax.dynamic_slice_in_dim(terms, target * cols, cols, terms.ndim - 1)
        total = total + within_layer(piece, section, k, n_feat).astype(jnp.float32)
    return total


def decode_scatter(features, decoder, feat_index, n_feat):
    cols = decoder.shape[1] // n_feat
    total = None
    anchor = None
    for k in sorted(range(n_feat), key=lambda shift: (-min(shift, n_feat - shift), shift)):
        target = (feat_index + k) % n_feat
        chunk = lax.dynamic_slice_in_dim(decoder, target * cols, cols, 1)
        piece = jnp.dot(features, chunk, preferred_element_type=jnp.float32).astype(jnp.bfloat16)
        anchor = piece[0, 0] if anchor is None else anchor + piece[0, 0]
        if k:
            piece = within_layer(piece, None, k, n_feat)
        else:
            piece = lax.optimization_barrier(piece)
        piece = piece.astype(jnp.float32)
        total = piece if total is None else total + piece
    return total, anchor


def feature_mask(block_list, block_count, feat_index, blocks_dev):
    listed = block_list[0]
    in_use = jnp.arange(listed.shape[1], dtype=jnp.int32)[None, :] < block_count[0][:, None]
    own_blocks = feat_index * blocks_dev + jnp.arange(blocks_dev, dtype=jnp.int32)
    matches = (listed[:, None, :] == own_blocks[None, :, None]) & in_use[:, None, :]
    active = jnp.any(matches, axis=2).astype(jnp.float32)
    return jnp.repeat(jnp.repeat(active, TILE, axis=0), BLOCK, axis=1)


def encode(gathered, enc_weight, enc_bias, mask):
    preact = (
        jnp.dot(gathered, enc_weight[0], preferred_element_type=jnp.float32) + enc_bias[0][None, :]
    )
    return (jax.nn.relu(preact) * mask).astype(jnp.bfloat16)


def decode(features, full):
    return jnp.dot(features, full, preferred_element_type=jnp.float32).astype(jnp.bfloat16)


def shards(
    resid_in, attn_out, carry_in, enc_weight, enc_bias, dec_own, dec_next, block_list, block_count
):
    n_feat = lax.axis_size("feat")
    section_index = lax.axis_index("layer")
    feat_index = lax.axis_index("feat")
    blocks_dev = enc_weight.shape[2] // BLOCK
    first_core = section_index == 0
    own_full = lax.all_gather(dec_own[0], TOK, axis=1, tiled=True)
    next_full = lax.all_gather(dec_next[0], TOK, axis=1, tiled=True)
    mask = feature_mask(block_list, block_count, feat_index, blocks_dev)
    attention = attn_out[0].astype(jnp.float32)

    def encoded(source, section):
        return lax.cond(
            section_index == section,
            lambda inner: encode(inner, enc_weight, enc_bias, mask),
            lambda inner: jnp.zeros((inner.shape[0], enc_weight.shape[2]), jnp.bfloat16),
            source,
        )

    features_first = encoded(feat_gather(resid_in, 0, feat_index, n_feat), 0)
    own_first, _ = decode_scatter(features_first, own_full, feat_index, n_feat)
    recon_first = own_first + carry_in.astype(jnp.float32)
    residual_next = (resid_in.astype(jnp.float32) + attention + recon_first).astype(jnp.bfloat16)
    residual_next = lax.ppermute(residual_next, "layer", [(0, 1)])

    features_second = encoded(feat_gather(residual_next, 1, feat_index, n_feat), 1)
    own_second, own_piece = decode_scatter(features_second, own_full, feat_index, n_feat)

    features = jnp.where(first_core, features_first, features_second)
    features = features + (own_piece * 0).astype(features.dtype)
    next_part, _ = decode_scatter(features, next_full, feat_index, n_feat)
    outgoing_now = next_part.astype(jnp.bfloat16)
    incoming = lax.ppermute(outgoing_now, "layer", [(0, 1)])
    recon_second = own_second + incoming.astype(jnp.float32)

    recon_out = jnp.where(first_core, recon_first, recon_second).astype(jnp.bfloat16)
    return (recon_out[None], outgoing_now[None])


def solution(mesh):
    devices = mesh.devices
    n_y = len({device.coords[1] for device in devices.reshape(-1)})
    split_mesh = Mesh(
        devices.reshape(devices.shape[:2] + (devices.shape[2] // n_y, n_y)),
        ("layer", "feat", "tz", "ty"),
    )
    return jax.shard_map(
        shards,
        mesh=split_mesh,
        in_specs=(
            P(TOK, "feat"),
            P("layer", TOK, "feat"),
            P(TOK, "feat"),
            P("layer", None, "feat"),
            P("layer", "feat"),
            P("layer", "feat", TOK),
            P("layer", "feat", TOK),
            P("layer", TOK, None),
            P("layer", TOK),
        ),
        out_specs=(P("layer", TOK, "feat"), P("layer", TOK, "feat")),
        check_vma=False,
    )
```
